512 devices in a mesh: dp: 16 (over x_lo, y), space: 32 (over x_hi, z, core).
Axes of the slice: x: 4 (x_hi: 2, x_lo: 2; x = x_hi * 2 + x_lo), y: 8, z: 8, core: 2. Of those that a mesh axis runs over, the one named last changes fastest.
Arguments:
- inputs: bfloat16 [16, 10, 64, 32, 128], P('dp', None, 'space'), may hold values from -8 to 8
- land_mask: int32 [16, 10, 64, 32], P('dp', None, 'space'), may hold values 0 or 1
- weight_one: float32 [128, 27, 128], P('dp'), may hold values from -0.109375 to 0.109375
- weight_two: float32 [128, 27, 128], P('dp'), may hold values from -0.109375 to 0.109375
- cotangent: bfloat16 [16, 10, 64, 32, 128], P('dp', None, 'space'), may hold values from -6 to 6
Outputs:
- prediction: bfloat16 [16, 10, 64, 32, 128], P('dp', None, 'space')
- input_grad: bfloat16 [16, 10, 64, 32, 128], P('dp', None, 'space')
- grad_one: float32 [128, 27, 128], P('dp')
- grad_two: float32 [128, 27, 128], P('dp')
The draws below stay inside these ranges and needn't reach their ends.
All inputs are finite; a program needn't handle non-finite values. No bound on the sum of `land_mask` on one device may be relied on, other than what follows from the above.
Results may differ from the reference program's by a relative error of at most 0.0067.
Values may be sent and summed in bfloat16 or wider, within the bound.
No kernel may reach another device: no remote copies, remote signals or barrier semaphores. Data moves between devices by JAX's collectives and lax.ppermute only.
A program may use at most 64 MiB of HBM per device.

```python
import jax
import jax.numpy as jnp

C = 128
TAPS = 27
DEPTH = 10
COLS = 32
SAMPLES = 16
ROWS = 64


def place_ends(values, stream_key, least, largest):
    longest = values.shape.index(max(values.shape))
    spots = []
    for shift in (0, 1):
        where = [jax.random.randint(jax.random.fold_in(stream_key, axis), (), 0, length) for axis, length in enumerate(values.shape)]
        where[longest] = (where[longest] + shift) % values.shape[longest]
        spots.append(tuple(where))
    return values.at[spots[0]].set(least).at[spots[1]].set(largest)


def spiked(drawn, own_key, source, target, parts, factor):
    def block_of(axis_at):
        return (jnp.arange(drawn.shape[axis_at]) // (drawn.shape[axis_at] // parts)).reshape((-1,) + (1,) * (drawn.ndim - 1 - axis_at))

    first = jax.random.permutation(own_key, parts)[block_of(target)]
    other_side = (block_of(target) + parts // 2) % parts
    return jnp.where((block_of(source) == first) | (block_of(source) == other_side), factor * drawn, drawn)


def shard_levels(own_key, extent, shards, smallest, largest):
    def one(position, parts):
        steps = jax.random.uniform(jax.random.fold_in(jax.random.fold_in(own_key, 6), position), (parts,), jnp.float32, smallest / len(shards), largest / len(shards))
        return jnp.repeat(jnp.exp(steps), extent[position] // parts).reshape((-1,) + (1,) * (len(extent) - position - 1))

    factor_of = one(*shards[0])
    for cut in shards[1:]:
        factor_of = factor_of * one(*cut)
    return factor_of


def gaussian(rng, dims, spread, limit, pieces=(), dtype=jnp.bfloat16):
    array = spread * jax.random.normal(rng, dims, jnp.float32)
    if pieces:
        array = array * shard_levels(rng, dims, pieces, -0.22, 0.18)
    return jnp.clip(array, -limit, limit).astype(dtype)


def bell_draw_with(stream_key, extent, scale, most, shards, heavy, kind=jnp.bfloat16):
    array = scale * jax.random.normal(stream_key, extent, jnp.float32)
    if shards:
        array = array * shard_levels(stream_key, extent, shards, -0.22, 0.18)
    return jnp.clip(spiked(array, jax.random.fold_in(stream_key, 3), *heavy), -most, most).astype(kind)


def setup_inputs(seed: int = 0) -> dict:
    splits = jax.random.split(jax.random.key(seed), 6)
    inputs = bell_draw_with(splits[0], (SAMPLES, DEPTH, ROWS, COLS, C), 1.0, 8.0, ((0, 16), (2, 32)), (0, 4, 16, 2.0))
    land_mask = place_ends((jax.random.randint(splits[1], (SAMPLES, DEPTH, ROWS, COLS), 0, 4) < 3).astype(jnp.int32), jax.random.fold_in(splits[1], 1), 0, 1)
    weight_one = gaussian(splits[2], (C, TAPS, C), (TAPS * C) ** -0.5, 0.109375, ((0, 16),), jnp.float32)
    weight_two = gaussian(splits[3], (C, TAPS, C), (TAPS * C) ** -0.5, 0.109375, ((0, 16),), jnp.float32)
    cotangent = gaussian(splits[4], (SAMPLES, DEPTH, ROWS, COLS, C), 1.0, 6.0, ((0, 16), (2, 32)))
    return dict(inputs=inputs, land_mask=land_mask, weight_one=weight_one, weight_two=weight_two, cotangent=cotangent)


def tap_offsets():
    return [(depth_off, row_off, col_off) for depth_off in range(3) for row_off in range(3) for col_off in range(3)]

def pad_cells(field):
    return jnp.pad(field, ((0, 0), (1, 1), (1, 1), (1, 1), (0, 0)))

def window_at(padded, offsets, shape):
    depth, rows, columns = shape
    return padded[:, offsets[0]:offsets[0] + depth, offsets[1]:offsets[1] + rows, offsets[2]:offsets[2] + columns, :].reshape(-1, padded.shape[4])

def forward_conv(padded, kernel, shape):
    total = None
    for number, offsets in enumerate(tap_offsets()):
        term = jnp.dot(window_at(padded, offsets, shape), kernel[:, number, :], preferred_element_type=jnp.float32)
        total = term if total is None else total + term
    return total

def transpose_conv(padded, kernel, shape):
    total = None
    for number, offsets in enumerate(tap_offsets()):
        mirror = (2 - offsets[0], 2 - offsets[1], 2 - offsets[2])
        term = jnp.dot(window_at(padded, mirror, shape), kernel[:, number, :].T, preferred_element_type=jnp.float32)
        total = term if total is None else total + term
    return total

def weight_grad(padded, back_flat, shape):
    terms = []
    for offsets in tap_offsets():
        terms.append(jnp.dot(window_at(padded, offsets, shape).T, back_flat, preferred_element_type=jnp.float32))
    return jnp.stack(terms, axis=1)

def reference(inputs, land_mask, weight_one, weight_two, cotangent):
    samples, depth, rows, columns, channel = inputs.shape
    shape = (depth, rows, columns)
    kernel_one = weight_one.astype(jnp.bfloat16)
    kernel_two = weight_two.astype(jnp.bfloat16)
    scale = land_mask.reshape(-1, 1).astype(jnp.float32)
    in_pad = pad_cells(inputs)
    pre_one = forward_conv(in_pad, kernel_one, shape)
    act_one = (scale * jax.nn.silu(pre_one)).astype(jnp.bfloat16).reshape(inputs.shape)
    act_pad = pad_cells(act_one)
    prediction = (scale * forward_conv(act_pad, kernel_two, shape)).astype(jnp.bfloat16).reshape(inputs.shape)
    back_two = (cotangent.reshape(-1, channel).astype(jnp.float32) * scale).astype(jnp.bfloat16)
    grad_two = weight_grad(act_pad, back_two, shape)
    pull_one = transpose_conv(pad_cells(back_two.reshape(inputs.shape)), kernel_two, shape)
    sigma = jax.nn.sigmoid(pre_one)
    back_one = (pull_one * scale * sigma * (1.0 + pre_one * (1.0 - sigma))).astype(jnp.bfloat16)
    grad_one = weight_grad(in_pad, back_one, shape)
    input_grad = transpose_conv(pad_cells(back_one.reshape(inputs.shape)), kernel_one, shape).astype(jnp.bfloat16).reshape(inputs.shape)
    return (prediction, input_grad, grad_one, grad_two)
```

```python
import jax
import jax.numpy as jnp
from jax import lax
from jax.sharding import PartitionSpec as P

HALO = 2
SPATIAL = ("NDHWC", "DHWIO", "NDHWC")


def exchange_rows(cells, width):
    count = lax.axis_size("space")
    ends = count - 1
    rows = cells.shape[2]
    head = lax.slice_in_dim(cells, 0, width, axis=2)
    tail = lax.slice_in_dim(cells, rows - width, rows, axis=2)
    above = lax.ppermute(tail, "space", [(i, i + 1) for i in range(ends)])
    below = lax.ppermute(head, "space", [(i + 1, i) for i in range(ends)])
    return jnp.concatenate([above, cells, below], axis=2)


def pad_depth_cols(field):
    return jnp.pad(field, ((0, 0), (1, 1), (0, 0), (1, 1), (0, 0)))


def conv(padded, kernel):
    return lax.conv_general_dilated(
        padded, kernel, (1, 1, 1), "VALID", dimension_numbers=SPATIAL,
        preferred_element_type=jnp.float32,
    )


def weight_grad(padded, back):
    out = lax.conv_general_dilated(
        padded, back, (1, 1, 1), "VALID", dimension_numbers=("CDHWN", "IDHWO", "NDHWC"),
        preferred_element_type=jnp.float32,
    )
    return out.reshape(out.shape[0], 27, out.shape[4])


def gather_kernel(weight):
    count = lax.axis_size("dp")
    local = weight.astype(jnp.bfloat16)
    copies = jnp.broadcast_to(local[None], (count,) + local.shape)
    full = lax.all_to_all(copies, "dp", 0, 0).reshape((-1,) + local.shape[1:])
    channel = full.shape[0]
    forward = jnp.transpose(full.reshape(channel, 3, 3, 3, full.shape[2]), (1, 2, 3, 0, 4))
    backward = jnp.transpose(forward[::-1, ::-1, ::-1], (0, 1, 2, 4, 3))
    return forward, backward


def reduce_grad(grad_full):
    count = lax.axis_size("dp")
    parts = grad_full.reshape((count, -1) + grad_full.shape[1:])
    owned = lax.all_to_all(parts, "dp", 0, 0).sum(axis=0)
    size = lax.axis_size("space")
    step = 1
    while step < size:
        owned = owned + lax.ppermute(owned, "space", [(i, i ^ step) for i in range(size)])
        step *= 2
    return owned


def on_device(inputs, land_mask, weight_one, weight_two, cotangent):
    rows = inputs.shape[2]
    channel = inputs.shape[4]
    mask = land_mask.astype(jnp.bfloat16)[..., None]
    back_two = (cotangent.astype(jnp.float32) * mask.astype(jnp.float32)).astype(jnp.bfloat16)
    both = exchange_rows(jnp.concatenate([inputs, back_two], axis=4), HALO)
    mask_wide = exchange_rows(mask, HALO).astype(jnp.float32)
    in_wide = both[..., :channel]
    back_two_wide = both[..., channel:]
    mask_mid = mask_wide[:, :, 1 : rows + 3]
    mask_own = mask_wide[:, :, 2 : rows + 2]

    k1, k1_t = gather_kernel(weight_one)
    k2, k2_t = gather_kernel(weight_two)

    pre_one = conv(pad_depth_cols(in_wide), k1)
    sigma = jax.nn.sigmoid(pre_one)
    act_one = (mask_mid * (pre_one * sigma)).astype(jnp.bfloat16)
    act_pad = pad_depth_cols(act_one)
    prediction = (mask_own * conv(act_pad, k2)).astype(jnp.bfloat16)

    back_own = back_two_wide[:, :, HALO : HALO + rows]
    grad_two = reduce_grad(weight_grad(act_pad, back_own))

    pull_one = conv(pad_depth_cols(back_two_wide), k2_t)
    back_one = (pull_one * mask_mid * sigma * (1.0 + pre_one * (1.0 - sigma))).astype(jnp.bfloat16)
    in_mid = pad_depth_cols(in_wide[:, :, 1 : rows + 3])
    grad_one = reduce_grad(weight_grad(in_mid, back_one[:, :, 1 : rows + 1]))
    input_grad = conv(pad_depth_cols(back_one), k1_t).astype(jnp.bfloat16)
    return (prediction, input_grad, grad_one, grad_two)


def solution(mesh):
    in_specs = (
        P("dp", None, "space", None, None),
        P("dp", None, "space", None),
        P("dp", None, None),
        P("dp", None, None),
        P("dp", None, "space", None, None),
    )
    out_specs = (
        P("dp", None, "space", None, None),
        P("dp", None, "space", None, None),
        P("dp", None, None),
        P("dp", None, None),
    )
    return jax.shard_map(
        on_device, mesh=mesh, in_specs=in_specs, out_specs=out_specs, check_vma=False
    )
```

```python
import jax
import jax.numpy as jnp
from jax import lax
from jax.sharding import PartitionSpec as P

HALO = 2
SPATIAL = ("NDHWC", "DHWIO", "NDHWC")


def exchange_rows(cells, width):
    count = lax.axis_size("space")
    ends = count - 1
    rows = cells.shape[2]
    head = lax.slice_in_dim(cells, 0, width, axis=2)
    tail = lax.slice_in_dim(cells, rows - width, rows, axis=2)
    above = lax.ppermute(tail, "space", [(i, i + 1) for i in range(ends)])
    below = lax.ppermute(head, "space", [(i + 1, i) for i in range(ends)])
    return jnp.concatenate([above, cells, below], axis=2)


def pad_depth_cols(field):
    return jnp.pad(field, ((0, 0), (1, 1), (0, 0), (1, 1), (0, 0)))


def conv(padded, kernel):
    return lax.conv_general_dilated(
        padded, kernel, (1, 1, 1), "VALID", dimension_numbers=SPATIAL,
        preferred_element_type=jnp.float32,
    )


def weight_grad(padded, back):
    out = lax.conv_general_dilated(
        padded, back, (1, 1, 1), "VALID", dimension_numbers=("CDHWN", "IDHWO", "NDHWC"),
        preferred_element_type=jnp.float32,
    )
    return out.reshape(out.shape[0], 27, out.shape[4])


def gather_kernel(weight):
    count = lax.axis_size("dp")
    local = weight.astype(jnp.bfloat16)
    copies = jnp.broadcast_to(local[None], (count,) + local.shape)
    full = lax.all_to_all(copies, "dp", 0, 0).reshape((-1,) + local.shape[1:])
    channel = full.shape[0]
    forward = jnp.transpose(full.reshape(channel, 3, 3, 3, full.shape[2]), (1, 2, 3, 0, 4))
    backward = jnp.transpose(forward[::-1, ::-1, ::-1], (0, 1, 2, 4, 3))
    return forward, backward


def reduce_grads(grads):
    count = lax.axis_size("dp")
    size = lax.axis_size("space")
    parts = jnp.stack([g.reshape((count, -1) + g.shape[1:]) for g in grads], axis=1)
    owned = lax.all_to_all(parts.astype(jnp.bfloat16), "dp", 0, 0)
    owned = owned.astype(jnp.float32).sum(axis=0)
    pieces = lax.all_to_all(owned.reshape(size, -1), "space", 0, 0).sum(axis=0)
    copies = jnp.broadcast_to(pieces[None], (size,) + pieces.shape)
    full = lax.all_to_all(copies, "space", 0, 0).reshape(owned.shape)
    return [full[i] for i in range(len(grads))]


def on_device(inputs, land_mask, weight_one, weight_two, cotangent):
    rows = inputs.shape[2]
    channel = inputs.shape[4]
    mask = land_mask.astype(jnp.bfloat16)[..., None]
    back_two = (cotangent.astype(jnp.float32) * mask.astype(jnp.float32)).astype(jnp.bfloat16)
    both = exchange_rows(jnp.concatenate([inputs, back_two], axis=4), HALO)
    mask_wide = exchange_rows(mask, HALO).astype(jnp.float32)
    in_wide = both[..., :channel]
    back_two_wide = both[..., channel:]
    mask_mid = mask_wide[:, :, 1 : rows + 3]
    mask_own = mask_wide[:, :, 2 : rows + 2]

    k1, k1_t = gather_kernel(weight_one)
    k2, k2_t = gather_kernel(weight_two)

    pre_one = conv(pad_depth_cols(in_wide), k1)
    sigma = jax.nn.sigmoid(pre_one)
    act_one = (mask_mid * (pre_one * sigma)).astype(jnp.bfloat16)
    act_pad = pad_depth_cols(act_one)
    prediction = (mask_own * conv(act_pad, k2)).astype(jnp.bfloat16)

    back_own = back_two_wide[:, :, HALO : HALO + rows]
    grad_two_terms = weight_grad(act_pad, back_own)

    pull_one = conv(pad_depth_cols(back_two_wide), k2_t)
    back_one = (pull_one * mask_mid * sigma * (1.0 + pre_one * (1.0 - sigma))).astype(jnp.bfloat16)
    in_mid = pad_depth_cols(in_wide[:, :, 1 : rows + 3])
    grad_one_terms = weight_grad(in_mid, back_one[:, :, 1 : rows + 1])
    grad_one, grad_two = reduce_grads([grad_one_terms, grad_two_terms])
    input_grad = conv(pad_depth_cols(back_one), k1_t).astype(jnp.bfloat16)
    return (prediction, input_grad, grad_one, grad_two)


def solution(mesh):
    in_specs = (
        P("dp", None, "space", None, None),
        P("dp", None, "space", None),
        P("dp", None, None),
        P("dp", None, None),
        P("dp", None, "space", None, None),
    )
    out_specs = (
        P("dp", None, "space", None, None),
        P("dp", None, "space", None, None),
        P("dp", None, None),
        P("dp", None, None),
    )
    return jax.shard_map(
        on_device, mesh=mesh, in_specs=in_specs, out_specs=out_specs, check_vma=False
    )
```

```python
import jax
import jax.numpy as jnp
from jax import lax
from jax.sharding import PartitionSpec as P

HALO = 2
SPATIAL = ("NDHWC", "DHWIO", "NDHWC")


def exchange_rows(cells, width):
    count = lax.axis_size("space")
    ends = count - 1
    rows = cells.shape[2]
    head = lax.slice_in_dim(cells, 0, width, axis=2)
    tail = lax.slice_in_dim(cells, rows - width, rows, axis=2)
    above = lax.ppermute(tail, "space", [(i, i + 1) for i in range(ends)])
    below = lax.ppermute(head, "space", [(i + 1, i) for i in range(ends)])
    return jnp.concatenate([above, cells, below], axis=2)


def pad_depth_cols(field):
    return jnp.pad(field, ((0, 0), (1, 1), (0, 0), (1, 1), (0, 0)))


def conv(padded, kernel):
    return lax.conv_general_dilated(
        padded, kernel, (1, 1, 1), "VALID", dimension_numbers=SPATIAL,
        preferred_element_type=jnp.float32,
    )


def weight_grad(padded, back):
    out = lax.conv_general_dilated(
        padded, back, (1, 1, 1), "VALID", dimension_numbers=("CDHWN", "IDHWO", "NDHWC"),
        preferred_element_type=jnp.float32,
    )
    return out.reshape(out.shape[0], 27, out.shape[4])


def gather_kernel(weight):
    count = lax.axis_size("dp")
    local = weight.astype(jnp.bfloat16)
    copies = jnp.broadcast_to(local[None], (count,) + local.shape)
    full = lax.all_to_all(copies, "dp", 0, 0).reshape((-1,) + local.shape[1:])
    channel = full.shape[0]
    forward = jnp.transpose(full.reshape(channel, 3, 3, 3, full.shape[2]), (1, 2, 3, 0, 4))
    backward = jnp.transpose(forward[::-1, ::-1, ::-1], (0, 1, 2, 4, 3))
    return forward, backward


def reduce_grads(grads):
    count = lax.axis_size("dp")
    size = lax.axis_size("space")
    me = lax.axis_index("space")
    core = me % 2
    rows = grads[0].shape[0] // count
    parts = jnp.stack([g.reshape((count, 2, rows // 2) + g.shape[1:]) for g in grads], axis=1)
    keep = lax.dynamic_index_in_dim(parts, core, axis=2, keepdims=False)
    send = lax.dynamic_index_in_dim(parts, 1 - core, axis=2, keepdims=False)
    mine = keep + lax.ppermute(send, "space", [(i, i ^ 1) for i in range(size)])
    owned = lax.all_to_all(mine.astype(jnp.bfloat16), "dp", 0, 0).astype(jnp.float32).sum(axis=0)
    pairs = size // 2
    pieces = owned.reshape(pairs, -1)
    spread = jnp.repeat(pieces, 2, axis=0)
    got = lax.all_to_all(spread, "space", 0, 0).reshape(pairs, 2, -1)
    piece = lax.dynamic_index_in_dim(got, core, axis=1, keepdims=False).sum(axis=0)
    copies = jnp.broadcast_to(piece[None], (size,) + piece.shape)
    full = lax.all_to_all(copies, "space", 0, 0).reshape(pairs, 2, -1)
    halves = jnp.transpose(full, (1, 0, 2)).reshape((2,) + owned.shape)
    joined = jnp.transpose(halves, (1, 0, 2, 3, 4)).reshape((len(grads), rows) + grads[0].shape[1:])
    return [joined[i] for i in range(len(grads))]


def on_device(inputs, land_mask, weight_one, weight_two, cotangent):
    rows = inputs.shape[2]
    channel = inputs.shape[4]
    mask = land_mask.astype(jnp.bfloat16)[..., None]
    back_two = (cotangent.astype(jnp.float32) * mask.astype(jnp.float32)).astype(jnp.bfloat16)
    both = exchange_rows(jnp.concatenate([inputs, back_two], axis=4), HALO)
    mask_wide = exchange_rows(mask, HALO).astype(jnp.float32)
    in_wide = both[..., :channel]
    back_two_wide = both[..., channel:]
    mask_mid = mask_wide[:, :, 1 : rows + 3]
    mask_own = mask_wide[:, :, 2 : rows + 2]

    k1, k1_t = gather_kernel(weight_one)
    k2, k2_t = gather_kernel(weight_two)

    pre_one = conv(pad_depth_cols(in_wide), k1)
    sigma = jax.nn.sigmoid(pre_one)
    act_one = (mask_mid * (pre_one * sigma)).astype(jnp.bfloat16)
    act_pad = pad_depth_cols(act_one)
    prediction = (mask_own * conv(act_pad, k2)).astype(jnp.bfloat16)

    back_own = back_two_wide[:, :, HALO : HALO + rows]
    grad_two_terms = weight_grad(act_pad, back_own)

    pull_one = conv(pad_depth_cols(back_two_wide), k2_t)
    back_one = (pull_one * mask_mid * sigma * (1.0 + pre_one * (1.0 - sigma))).astype(jnp.bfloat16)
    in_mid = pad_depth_cols(in_wide[:, :, 1 : rows + 3])
    grad_one_terms = weight_grad(in_mid, back_one[:, :, 1 : rows + 1])
    grad_one, grad_two = reduce_grads([grad_one_terms, grad_two_terms])
    input_grad = conv(pad_depth_cols(back_one), k1_t).astype(jnp.bfloat16)
    return (prediction, input_grad, grad_one, grad_two)


def solution(mesh):
    in_specs = (
        P("dp", None, "space", None, None),
        P("dp", None, "space", None),
        P("dp", None, None),
        P("dp", None, None),
        P("dp", None, "space", None, None),
    )
    out_specs = (
        P("dp", None, "space", None, None),
        P("dp", None, "space", None, None),
        P("dp", None, None),
        P("dp", None, None),
    )
    return jax.shard_map(
        on_device, mesh=mesh, in_specs=in_specs, out_specs=out_specs, check_vma=False
    )
```

```python
import jax
import jax.numpy as jnp
from jax import lax
from jax.sharding import PartitionSpec as P

HALO = 2
SPATIAL = ("NDHWC", "DHWIO", "NDHWC")


def exchange_rows(cells, width):
    count = lax.axis_size("space")
    ends = count - 1
    rows = cells.shape[2]
    head = lax.slice_in_dim(cells, 0, width, axis=2)
    tail = lax.slice_in_dim(cells, rows - width, rows, axis=2)
    above = lax.ppermute(tail, "space", [(i, i + 1) for i in range(ends)])
    below = lax.ppermute(head, "space", [(i + 1, i) for i in range(ends)])
    return jnp.concatenate([above, cells, below], axis=2)


def pad_depth_cols(field):
    return jnp.pad(field, ((0, 0), (1, 1), (0, 0), (1, 1), (0, 0)))


def conv(padded, kernel):
    return lax.conv_general_dilated(
        padded, kernel, (1, 1, 1), "VALID", dimension_numbers=SPATIAL,
        preferred_element_type=jnp.float32,
    )


def weight_grad(padded, back):
    out = lax.conv_general_dilated(
        padded, back, (1, 1, 1), "VALID", dimension_numbers=("CDHWN", "IDHWO", "NDHWC"),
        preferred_element_type=jnp.float32,
    )
    return out.reshape(out.shape[0], 27, out.shape[4])


def gather_kernel(weight):
    count = lax.axis_size("dp")
    size = lax.axis_size("space")
    core = lax.axis_index("space") % 2
    rows = weight.shape[0]
    local = weight.astype(jnp.bfloat16).reshape((2, rows // 2) + weight.shape[1:])
    half = lax.dynamic_index_in_dim(local, core, axis=0, keepdims=False)
    copies = jnp.broadcast_to(half[None], (count,) + half.shape)
    mine = lax.all_to_all(copies, "dp", 0, 0)
    theirs = lax.ppermute(mine, "space", [(i, i ^ 1) for i in range(size)])
    first = jnp.where(core == 0, mine, theirs)
    second = jnp.where(core == 0, theirs, mine)
    full = jnp.stack([first, second], axis=1).reshape((count * rows,) + weight.shape[1:])
    channel = full.shape[0]
    forward = jnp.transpose(full.reshape(channel, 3, 3, 3, full.shape[2]), (1, 2, 3, 0, 4))
    backward = jnp.transpose(forward[::-1, ::-1, ::-1], (0, 1, 2, 4, 3))
    return forward, backward


def reduce_grads(grads):
    count = lax.axis_size("dp")
    size = lax.axis_size("space")
    me = lax.axis_index("space")
    core = me % 2
    rows = grads[0].shape[0] // count
    parts = jnp.stack([g.reshape((count, 2, rows // 2) + g.shape[1:]) for g in grads], axis=1)
    keep = lax.dynamic_index_in_dim(parts, core, axis=2, keepdims=False)
    send = lax.dynamic_index_in_dim(parts, 1 - core, axis=2, keepdims=False)
    mine = keep + lax.ppermute(send, "space", [(i, i ^ 1) for i in range(size)])
    owned = lax.all_to_all(mine.astype(jnp.bfloat16), "dp", 0, 0).astype(jnp.float32).sum(axis=0)
    pairs = size // 2
    pieces = owned.reshape(pairs, -1)
    spread = jnp.repeat(pieces, 2, axis=0)
    got = lax.all_to_all(spread, "space", 0, 0).reshape(pairs, 2, -1)
    piece = lax.dynamic_index_in_dim(got, core, axis=1, keepdims=False).sum(axis=0)
    copies = jnp.broadcast_to(piece[None], (size,) + piece.shape)
    full = lax.all_to_all(copies, "space", 0, 0).reshape(pairs, 2, -1)
    halves = jnp.transpose(full, (1, 0, 2)).reshape((2,) + owned.shape)
    joined = jnp.transpose(halves, (1, 0, 2, 3, 4)).reshape((len(grads), rows) + grads[0].shape[1:])
    return [joined[i] for i in range(len(grads))]


def on_device(inputs, land_mask, weight_one, weight_two, cotangent):
    rows = inputs.shape[2]
    channel = inputs.shape[4]
    mask = land_mask.astype(jnp.bfloat16)[..., None]
    back_two = (cotangent.astype(jnp.float32) * mask.astype(jnp.float32)).astype(jnp.bfloat16)
    both = exchange_rows(jnp.concatenate([inputs, back_two], axis=4), HALO)
    mask_wide = exchange_rows(mask, HALO).astype(jnp.float32)
    in_wide = both[..., :channel]
    back_two_wide = both[..., channel:]
    mask_mid = mask_wide[:, :, 1 : rows + 3]
    mask_own = mask_wide[:, :, 2 : rows + 2]

    k1, k1_t = gather_kernel(weight_one)
    k2, k2_t = gather_kernel(weight_two)

    pre_one = conv(pad_depth_cols(in_wide), k1)
    sigma = jax.nn.sigmoid(pre_one)
    act_one = (mask_mid * (pre_one * sigma)).astype(jnp.bfloat16)
    act_pad = pad_depth_cols(act_one)
    prediction = (mask_own * conv(act_pad, k2)).astype(jnp.bfloat16)

    back_own = back_two_wide[:, :, HALO : HALO + rows]
    grad_two_terms = weight_grad(act_pad, back_own)

    pull_one = conv(pad_depth_cols(back_two_wide), k2_t)
    back_one = (pull_one * mask_mid * sigma * (1.0 + pre_one * (1.0 - sigma))).astype(jnp.bfloat16)
    in_mid = pad_depth_cols(in_wide[:, :, 1 : rows + 3])
    grad_one_terms = weight_grad(in_mid, back_one[:, :, 1 : rows + 1])
    grad_one, grad_two = reduce_grads([grad_one_terms, grad_two_terms])
    input_grad = conv(pad_depth_cols(back_one), k1_t).astype(jnp.bfloat16)
    return (prediction, input_grad, grad_one, grad_two)


def solution(mesh):
    in_specs = (
        P("dp", None, "space", None, None),
        P("dp", None, "space", None),
        P("dp", None, None),
        P("dp", None, None),
        P("dp", None, "space", None, None),
    )
    out_specs = (
        P("dp", None, "space", None, None),
        P("dp", None, "space", None, None),
        P("dp", None, None),
        P("dp", None, None),
    )
    return jax.shard_map(
        on_device, mesh=mesh, in_specs=in_specs, out_specs=out_specs, check_vma=False
    )
```

```python
import jax
import jax.numpy as jnp
from jax import lax
from jax.sharding import PartitionSpec as P

HALO = 2
SPATIAL = ("NDHWC", "DHWIO", "NDHWC")


def exchange_rows(cells, width):
    count = lax.axis_size("space")
    ends = count - 1
    rows = cells.shape[2]
    head = lax.slice_in_dim(cells, 0, width, axis=2)
    tail = lax.slice_in_dim(cells, rows - width, rows, axis=2)
    above = lax.ppermute(tail, "space", [(i, i + 1) for i in range(ends)])
    below = lax.ppermute(head, "space", [(i + 1, i) for i in range(ends)])
    return jnp.concatenate([above, cells, below], axis=2)


def pad_depth_cols(field):
    return jnp.pad(field, ((0, 0), (1, 1), (0, 0), (1, 1), (0, 0)))


def conv(padded, kernel):
    return lax.conv_general_dilated(
        padded, kernel, (1, 1, 1), "VALID", dimension_numbers=SPATIAL,
        preferred_element_type=jnp.float32,
    )


def weight_grad(padded, back):
    out = lax.conv_general_dilated(
        padded, back, (1, 1, 1), "VALID", dimension_numbers=("CDHWN", "IDHWO", "NDHWC"),
        preferred_element_type=jnp.float32,
    )
    return out.reshape(out.shape[0], 27, out.shape[4])


def gather_kernel(weight):
    count = lax.axis_size("dp")
    local = weight.astype(jnp.bfloat16)
    copies = jnp.broadcast_to(local[None], (count,) + local.shape)
    full = lax.all_to_all(copies, "dp", 0, 0).reshape((-1,) + local.shape[1:])
    channel = full.shape[0]
    forward = jnp.transpose(full.reshape(channel, 3, 3, 3, full.shape[2]), (1, 2, 3, 0, 4))
    backward = jnp.transpose(forward[::-1, ::-1, ::-1], (0, 1, 2, 4, 3))
    return forward, backward


def gather_doubling(weight):
    count = lax.axis_size("dp")
    me = lax.axis_index("dp")
    local = weight.astype(jnp.bfloat16)
    held = local[None]
    order = []
    step = count // 4
    steps = []
    while step >= 1:
        steps.append(step)
        step //= 2
    steps.append(count // 2)
    for step in steps:
        got = lax.ppermute(held, "dp", [(i, i ^ step) for i in range(count)])
        low = (me // step) % 2 == 0
        held = jnp.where(low, jnp.concatenate([held, got]), jnp.concatenate([got, held]))
        order.append(step)
    blocks = [sum(step for j, step in enumerate(order) if (p >> j) & 1) for p in range(count)]
    where = [blocks.index(b) for b in range(count)]
    full = jnp.take(held, jnp.array(where), axis=0)
    full = full.reshape((-1,) + local.shape[1:])
    channel = full.shape[0]
    forward = jnp.transpose(full.reshape(channel, 3, 3, 3, full.shape[2]), (1, 2, 3, 0, 4))
    backward = jnp.transpose(forward[::-1, ::-1, ::-1], (0, 1, 2, 4, 3))
    return forward, backward


def reduce_grads(grads):
    count = lax.axis_size("dp")
    size = lax.axis_size("space")
    me = lax.axis_index("space")
    core = me % 2
    rows = grads[0].shape[0] // count
    parts = jnp.stack([g.reshape((count, 2, rows // 2) + g.shape[1:]) for g in grads], axis=1)
    keep = lax.dynamic_index_in_dim(parts, core, axis=2, keepdims=False)
    send = lax.dynamic_index_in_dim(parts, 1 - core, axis=2, keepdims=False)
    mine = keep + lax.ppermute(send, "space", [(i, i ^ 1) for i in range(size)])
    owned = lax.all_to_all(mine.astype(jnp.bfloat16), "dp", 0, 0).astype(jnp.float32).sum(axis=0)
    pairs = size // 2
    pieces = owned.reshape(pairs, -1)
    spread = jnp.repeat(pieces, 2, axis=0)
    got = lax.all_to_all(spread, "space", 0, 0).reshape(pairs, 2, -1)
    piece = lax.dynamic_index_in_dim(got, core, axis=1, keepdims=False).sum(axis=0)
    copies = jnp.broadcast_to(piece[None], (size,) + piece.shape)
    full = lax.all_to_all(copies, "space", 0, 0).reshape(pairs, 2, -1)
    halves = jnp.transpose(full, (1, 0, 2)).reshape((2,) + owned.shape)
    joined = jnp.transpose(halves, (1, 0, 2, 3, 4)).reshape((len(grads), rows) + grads[0].shape[1:])
    return [joined[i] for i in range(len(grads))]


def on_device(inputs, land_mask, weight_one, weight_two, cotangent):
    rows = inputs.shape[2]
    channel = inputs.shape[4]
    mask = land_mask.astype(jnp.bfloat16)[..., None]
    back_two = (cotangent.astype(jnp.float32) * mask.astype(jnp.float32)).astype(jnp.bfloat16)
    both = exchange_rows(jnp.concatenate([inputs, back_two], axis=4), HALO)
    mask_wide = exchange_rows(mask, HALO).astype(jnp.float32)
    in_wide = both[..., :channel]
    back_two_wide = both[..., channel:]
    mask_mid = mask_wide[:, :, 1 : rows + 3]
    mask_own = mask_wide[:, :, 2 : rows + 2]

    k1, k1_t = gather_kernel(weight_one)
    k2, k2_t = gather_doubling(weight_two)

    pre_one = conv(pad_depth_cols(in_wide), k1)
    sigma = jax.nn.sigmoid(pre_one)
    act_one = (mask_mid * (pre_one * sigma)).astype(jnp.bfloat16)
    act_pad = pad_depth_cols(act_one)
    prediction = (mask_own * conv(act_pad, k2)).astype(jnp.bfloat16)

    back_own = back_two_wide[:, :, HALO : HALO + rows]
    grad_two_terms = weight_grad(act_pad, back_own)

    pull_one = conv(pad_depth_cols(back_two_wide), k2_t)
    back_one = (pull_one * mask_mid * sigma * (1.0 + pre_one * (1.0 - sigma))).astype(jnp.bfloat16)
    in_mid = pad_depth_cols(in_wide[:, :, 1 : rows + 3])
    grad_one_terms = weight_grad(in_mid, back_one[:, :, 1 : rows + 1])
    grad_one, grad_two = reduce_grads([grad_one_terms, grad_two_terms])
    input_grad = conv(pad_depth_cols(back_one), k1_t).astype(jnp.bfloat16)
    return (prediction, input_grad, grad_one, grad_two)


def solution(mesh):
    in_specs = (
        P("dp", None, "space", None, None),
        P("dp", None, "space", None),
        P("dp", None, None),
        P("dp", None, None),
        P("dp", None, "space", None, None),
    )
    out_specs = (
        P("dp", None, "space", None, None),
        P("dp", None, "space", None, None),
        P("dp", None, None),
        P("dp", None, None),
    )
    return jax.shard_map(
        on_device, mesh=mesh, in_specs=in_specs, out_specs=out_specs, check_vma=False
    )
```

```python
import jax
import jax.numpy as jnp
from jax import lax
from jax.sharding import PartitionSpec as P

HALO = 2
SPATIAL = ("NDHWC", "DHWIO", "NDHWC")


def exchange_rows(cells, width):
    count = lax.axis_size("space")
    ends = count - 1
    rows = cells.shape[2]
    head = lax.slice_in_dim(cells, 0, width, axis=2)
    tail = lax.slice_in_dim(cells, rows - width, rows, axis=2)
    above = lax.ppermute(tail, "space", [(i, i + 1) for i in range(ends)])
    below = lax.ppermute(head, "space", [(i + 1, i) for i in range(ends)])
    return jnp.concatenate([above, cells, below], axis=2)


def pad_depth_cols(field):
    return jnp.pad(field, ((0, 0), (1, 1), (0, 0), (1, 1), (0, 0)))


def conv(padded, kernel):
    return lax.conv_general_dilated(
        padded, kernel, (1, 1, 1), "VALID", dimension_numbers=SPATIAL,
        preferred_element_type=jnp.float32,
    )


def weight_grad(padded, back):
    out = lax.conv_general_dilated(
        padded, back, (1, 1, 1), "VALID", dimension_numbers=("CDHWN", "IDHWO", "NDHWC"),
        preferred_element_type=jnp.float32,
    )
    return out.reshape(out.shape[0], 27, out.shape[4])


def gather_kernel(weight):
    count = lax.axis_size("dp")
    local = weight.astype(jnp.bfloat16)
    copies = jnp.broadcast_to(local[None], (count,) + local.shape)
    full = lax.all_to_all(copies, "dp", 0, 0).reshape((-1,) + local.shape[1:])
    channel = full.shape[0]
    forward = jnp.transpose(full.reshape(channel, 3, 3, 3, full.shape[2]), (1, 2, 3, 0, 4))
    backward = jnp.transpose(forward[::-1, ::-1, ::-1], (0, 1, 2, 4, 3))
    return forward, backward


def reduce_grads(grads):
    count = lax.axis_size("dp")
    size = lax.axis_size("space")
    me = lax.axis_index("space")
    core = me % 2
    rows = grads[0].shape[0] // count
    parts = jnp.stack([g.reshape((count, 2, rows // 2) + g.shape[1:]) for g in grads], axis=1)
    keep = lax.dynamic_index_in_dim(parts, core, axis=2, keepdims=False)
    send = lax.dynamic_index_in_dim(parts, 1 - core, axis=2, keepdims=False)
    mine = keep + lax.ppermute(send, "space", [(i, i ^ 1) for i in range(size)])
    owned = lax.all_to_all(mine.astype(jnp.bfloat16), "dp", 0, 0).astype(jnp.float32).sum(axis=0)
    pairs = size // 2
    pieces = owned.reshape(pairs, -1)
    spread = jnp.repeat(pieces, 2, axis=0)
    got = lax.all_to_all(spread, "space", 0, 0).reshape(pairs, 2, -1)
    piece = lax.dynamic_index_in_dim(got, core, axis=1, keepdims=False).sum(axis=0)
    copies = jnp.broadcast_to(piece[None], (size,) + piece.shape)
    full = lax.all_to_all(copies, "space", 0, 0).reshape(pairs, 2, -1)
    halves = jnp.transpose(full, (1, 0, 2)).reshape((2,) + owned.shape)
    joined = jnp.transpose(halves, (1, 0, 2, 3, 4)).reshape((len(grads), rows) + grads[0].shape[1:])
    return [joined[i] for i in range(len(grads))]


def on_device(inputs, land_mask, weight_one, weight_two, cotangent):
    rows = inputs.shape[2]
    channel = inputs.shape[4]
    mask = land_mask.astype(jnp.bfloat16)[..., None]
    back_two = (cotangent.astype(jnp.float32) * mask.astype(jnp.float32)).astype(jnp.bfloat16)
    both = exchange_rows(jnp.concatenate([inputs, back_two], axis=4), HALO)
    mask_wide = exchange_rows(mask, HALO).astype(jnp.float32)
    in_wide = both[..., :channel]
    back_two_wide = both[..., channel:]
    mask_mid = mask_wide[:, :, 1 : rows + 3]
    mask_own = mask_wide[:, :, 2 : rows + 2]

    k1, k1_t = gather_kernel(weight_one)
    k2, k2_t = gather_kernel(weight_two)

    pre_one = conv(pad_depth_cols(in_wide), k1)
    sigma = jax.nn.sigmoid(pre_one)
    act_one = (mask_mid * (pre_one * sigma)).astype(jnp.bfloat16)
    act_pad = pad_depth_cols(act_one)
    back_own = back_two_wide[:, :, HALO : HALO + rows]
    grad_two_terms = weight_grad(act_pad, back_own)
    grad_two_terms, k2, k2_t = lax.optimization_barrier((grad_two_terms, k2, k2_t))
    prediction = (mask_own * conv(act_pad, k2)).astype(jnp.bfloat16)

    pull_one = conv(pad_depth_cols(back_two_wide), k2_t)
    back_one = (pull_one * mask_mid * sigma * (1.0 + pre_one * (1.0 - sigma))).astype(jnp.bfloat16)
    in_mid = pad_depth_cols(in_wide[:, :, 1 : rows + 3])
    grad_one_terms = weight_grad(in_mid, back_one[:, :, 1 : rows + 1])
    grad_one, grad_two = reduce_grads([grad_one_terms, grad_two_terms])
    input_grad = conv(pad_depth_cols(back_one), k1_t).astype(jnp.bfloat16)
    return (prediction, input_grad, grad_one, grad_two)


def solution(mesh):
    in_specs = (
        P("dp", None, "space", None, None),
        P("dp", None, "space", None),
        P("dp", None, None),
        P("dp", None, None),
        P("dp", None, "space", None, None),
    )
    out_specs = (
        P("dp", None, "space", None, None),
        P("dp", None, "space", None, None),
        P("dp", None, None),
        P("dp", None, None),
    )
    return jax.shard_map(
        on_device, mesh=mesh, in_specs=in_specs, out_specs=out_specs, check_vma=False
    )
```

```python
import jax
import jax.numpy as jnp
from jax import lax
from jax.sharding import PartitionSpec as P

HALO = 2
SPATIAL = ("NDHWC", "DHWIO", "NDHWC")


def exchange_rows(cells, width):
    count = lax.axis_size("space")
    ends = count - 1
    rows = cells.shape[2]
    head = lax.slice_in_dim(cells, 0, width, axis=2)
    tail = lax.slice_in_dim(cells, rows - width, rows, axis=2)
    above = lax.ppermute(tail, "space", [(i, i + 1) for i in range(ends)])
    below = lax.ppermute(head, "space", [(i + 1, i) for i in range(ends)])
    return jnp.concatenate([above, cells, below], axis=2)


def pad_depth_cols(field):
    return jnp.pad(field, ((0, 0), (1, 1), (0, 0), (1, 1), (0, 0)))


def conv(padded, kernel):
    return lax.conv_general_dilated(
        padded, kernel, (1, 1, 1), "VALID", dimension_numbers=SPATIAL,
        preferred_element_type=jnp.float32,
    )


def weight_grad(padded, back):
    out = lax.conv_general_dilated(
        padded, back, (1, 1, 1), "VALID", dimension_numbers=("CDHWN", "IDHWO", "NDHWC"),
        preferred_element_type=jnp.float32,
    )
    return out.reshape(out.shape[0], 27, out.shape[4])


def gather_kernel(weight):
    count = lax.axis_size("dp")
    local = weight.astype(jnp.bfloat16)
    copies = jnp.broadcast_to(local[None], (count,) + local.shape)
    full = lax.all_to_all(copies, "dp", 0, 0).reshape((-1,) + local.shape[1:])
    channel = full.shape[0]
    forward = jnp.transpose(full.reshape(channel, 3, 3, 3, full.shape[2]), (1, 2, 3, 0, 4))
    backward = jnp.transpose(forward[::-1, ::-1, ::-1], (0, 1, 2, 4, 3))
    return forward, backward


def reduce_grads(grads):
    count = lax.axis_size("dp")
    size = lax.axis_size("space")
    me = lax.axis_index("space")
    core = me % 2
    rows = grads[0].shape[0] // count
    parts = jnp.stack([g.reshape((count, 2, rows // 2) + g.shape[1:]) for g in grads], axis=1)
    keep = lax.dynamic_index_in_dim(parts, core, axis=2, keepdims=False)
    send = lax.dynamic_index_in_dim(parts, 1 - core, axis=2, keepdims=False)
    mine = keep + lax.ppermute(send, "space", [(i, i ^ 1) for i in range(size)])
    owned = lax.all_to_all(mine.astype(jnp.bfloat16), "dp", 0, 0).astype(jnp.float32).sum(axis=0)
    pairs = size // 2
    pieces = owned.reshape(pairs, -1)
    spread = jnp.repeat(pieces, 2, axis=0)
    got = lax.all_to_all(spread, "space", 0, 0).reshape(pairs, 2, -1)
    piece = lax.dynamic_index_in_dim(got, core, axis=1, keepdims=False).sum(axis=0)
    copies = jnp.broadcast_to(piece[None], (size,) + piece.shape)
    full = lax.all_to_all(copies, "space", 0, 0).reshape(pairs, 2, -1)
    halves = jnp.transpose(full, (1, 0, 2)).reshape((2,) + owned.shape)
    joined = jnp.transpose(halves, (1, 0, 2, 3, 4)).reshape((len(grads), rows) + grads[0].shape[1:])
    return [joined[i] for i in range(len(grads))]


def on_device(inputs, land_mask, weight_one, weight_two, cotangent):
    rows = inputs.shape[2]
    channel = inputs.shape[4]
    mask = land_mask.astype(jnp.bfloat16)[..., None]
    back_two = (cotangent.astype(jnp.float32) * mask.astype(jnp.float32)).astype(jnp.bfloat16)
    both = exchange_rows(jnp.concatenate([inputs, back_two], axis=4), HALO)
    mask_wide = exchange_rows(mask, HALO).astype(jnp.float32)
    in_wide = both[..., :channel]
    back_two_wide = both[..., channel:]
    mask_mid = mask_wide[:, :, 1 : rows + 3]
    mask_own = mask_wide[:, :, 2 : rows + 2]

    k1, k1_t = gather_kernel(weight_one)
    k2, k2_t = gather_kernel(weight_two)

    pre_one = conv(pad_depth_cols(in_wide), k1)
    sigma = jax.nn.sigmoid(pre_one)
    act_one = (mask_mid * (pre_one * sigma)).astype(jnp.bfloat16)
    act_pad = pad_depth_cols(act_one)
    prediction = (mask_own * conv(act_pad, k2)).astype(jnp.bfloat16)

    back_own = back_two_wide[:, :, HALO : HALO + rows]
    grad_two_terms = weight_grad(act_pad, back_own)
    grad_two_terms, back_two_wide = lax.optimization_barrier((grad_two_terms, back_two_wide))

    pull_one = conv(pad_depth_cols(back_two_wide), k2_t)
    back_one = (pull_one * mask_mid * sigma * (1.0 + pre_one * (1.0 - sigma))).astype(jnp.bfloat16)
    in_mid = pad_depth_cols(in_wide[:, :, 1 : rows + 3])
    grad_one_terms = weight_grad(in_mid, back_one[:, :, 1 : rows + 1])
    grad_one, grad_two = reduce_grads([grad_one_terms, grad_two_terms])
    input_grad = conv(pad_depth_cols(back_one), k1_t).astype(jnp.bfloat16)
    return (prediction, input_grad, grad_one, grad_two)


def solution(mesh):
    in_specs = (
        P("dp", None, "space", None, None),
        P("dp", None, "space", None),
        P("dp", None, None),
        P("dp", None, None),
        P("dp", None, "space", None, None),
    )
    out_specs = (
        P("dp", None, "space", None, None),
        P("dp", None, "space", None, None),
        P("dp", None, None),
        P("dp", None, None),
    )
    return jax.shard_map(
        on_device, mesh=mesh, in_specs=in_specs, out_specs=out_specs, check_vma=False
    )
```

```python
import jax
import jax.numpy as jnp
from jax import lax
from jax.sharding import PartitionSpec as P

HALO = 2
SPATIAL = ("NDHWC", "DHWIO", "NDHWC")


def exchange_rows(cells, width):
    count = lax.axis_size("space")
    ends = count - 1
    rows = cells.shape[2]
    head = lax.slice_in_dim(cells, 0, width, axis=2)
    tail = lax.slice_in_dim(cells, rows - width, rows, axis=2)
    above = lax.ppermute(tail, "space", [(i, i + 1) for i in range(ends)])
    below = lax.ppermute(head, "space", [(i + 1, i) for i in range(ends)])
    return jnp.concatenate([above, cells, below], axis=2)


def pad_depth_cols(field):
    return jnp.pad(field, ((0, 0), (1, 1), (0, 0), (1, 1), (0, 0)))


def conv(padded, kernel):
    return lax.conv_general_dilated(
        padded, kernel, (1, 1, 1), "VALID", dimension_numbers=SPATIAL,
        preferred_element_type=jnp.float32,
    )


def weight_grad(padded, back):
    out = lax.conv_general_dilated(
        padded, back, (1, 1, 1), "VALID", dimension_numbers=("CDHWN", "IDHWO", "NDHWC"),
        preferred_element_type=jnp.float32,
    )
    return out.reshape(out.shape[0], 27, out.shape[4])


def gather_kernel(weight, issued=None):
    count = lax.axis_size("dp")
    local = weight.astype(jnp.bfloat16)
    copies = jnp.broadcast_to(local[None], (count,) + local.shape)
    if issued is not None:
        copies, issued = lax.optimization_barrier((copies, issued))
    full = lax.all_to_all(copies, "dp", 0, 0).reshape((-1,) + local.shape[1:])
    channel = full.shape[0]
    forward = jnp.transpose(full.reshape(channel, 3, 3, 3, full.shape[2]), (1, 2, 3, 0, 4))
    backward = jnp.transpose(forward[::-1, ::-1, ::-1], (0, 1, 2, 4, 3))
    if issued is not None:
        return forward, backward, issued
    return forward, backward


def reduce_grads(grads):
    count = lax.axis_size("dp")
    size = lax.axis_size("space")
    me = lax.axis_index("space")
    core = me % 2
    rows = grads[0].shape[0] // count
    parts = jnp.stack([g.reshape((count, 2, rows // 2) + g.shape[1:]) for g in grads], axis=1)
    keep = lax.dynamic_index_in_dim(parts, core, axis=2, keepdims=False)
    send = lax.dynamic_index_in_dim(parts, 1 - core, axis=2, keepdims=False)
    mine = keep + lax.ppermute(send, "space", [(i, i ^ 1) for i in range(size)])
    owned = lax.all_to_all(mine.astype(jnp.bfloat16), "dp", 0, 0).astype(jnp.float32).sum(axis=0)
    pairs = size // 2
    pieces = owned.reshape(pairs, -1)
    spread = jnp.repeat(pieces, 2, axis=0)
    got = lax.all_to_all(spread, "space", 0, 0).reshape(pairs, 2, -1)
    piece = lax.dynamic_index_in_dim(got, core, axis=1, keepdims=False).sum(axis=0)
    copies = jnp.broadcast_to(piece[None], (size,) + piece.shape)
    full = lax.all_to_all(copies, "space", 0, 0).reshape(pairs, 2, -1)
    halves = jnp.transpose(full, (1, 0, 2)).reshape((2,) + owned.shape)
    joined = jnp.transpose(halves, (1, 0, 2, 3, 4)).reshape((len(grads), rows) + grads[0].shape[1:])
    return [joined[i] for i in range(len(grads))]


def on_device(inputs, land_mask, weight_one, weight_two, cotangent):
    rows = inputs.shape[2]
    channel = inputs.shape[4]
    mask = land_mask.astype(jnp.bfloat16)[..., None]
    back_two = (cotangent.astype(jnp.float32) * mask.astype(jnp.float32)).astype(jnp.bfloat16)
    k1, k1_t, (rimmed, mask) = gather_kernel(weight_one, (jnp.concatenate([inputs, back_two], axis=4), mask))
    both = exchange_rows(rimmed, HALO)
    mask_wide = exchange_rows(mask, HALO).astype(jnp.float32)
    in_wide = both[..., :channel]
    back_two_wide = both[..., channel:]
    mask_mid = mask_wide[:, :, 1 : rows + 3]
    mask_own = mask_wide[:, :, 2 : rows + 2]

    k2, k2_t = gather_kernel(weight_two)

    pre_one = conv(pad_depth_cols(in_wide), k1)
    sigma = jax.nn.sigmoid(pre_one)
    act_one = (mask_mid * (pre_one * sigma)).astype(jnp.bfloat16)
    act_pad = pad_depth_cols(act_one)
    prediction = (mask_own * conv(act_pad, k2)).astype(jnp.bfloat16)

    back_own = back_two_wide[:, :, HALO : HALO + rows]
    grad_two_terms = weight_grad(act_pad, back_own)
    grad_two_terms, back_two_wide = lax.optimization_barrier((grad_two_terms, back_two_wide))

    pull_one = conv(pad_depth_cols(back_two_wide), k2_t)
    back_one = (pull_one * mask_mid * sigma * (1.0 + pre_one * (1.0 - sigma))).astype(jnp.bfloat16)
    in_mid = pad_depth_cols(in_wide[:, :, 1 : rows + 3])
    grad_one_terms = weight_grad(in_mid, back_one[:, :, 1 : rows + 1])
    grad_one, grad_two = reduce_grads([grad_one_terms, grad_two_terms])
    input_grad = conv(pad_depth_cols(back_one), k1_t).astype(jnp.bfloat16)
    return (prediction, input_grad, grad_one, grad_two)


def solution(mesh):
    in_specs = (
        P("dp", None, "space", None, None),
        P("dp", None, "space", None),
        P("dp", None, None),
        P("dp", None, None),
        P("dp", None, "space", None, None),
    )
    out_specs = (
        P("dp", None, "space", None, None),
        P("dp", None, "space", None, None),
        P("dp", None, None),
        P("dp", None, None),
    )
    return jax.shard_map(
        on_device, mesh=mesh, in_specs=in_specs, out_specs=out_specs, check_vma=False
    )
```

```python
import jax
import jax.numpy as jnp
from jax import lax
from jax.sharding import PartitionSpec as P

HALO = 2
SPATIAL = ("NDHWC", "DHWIO", "NDHWC")


def exchange_rows(cells, width):
    count = lax.axis_size("space")
    ends = count - 1
    rows = cells.shape[2]
    head = lax.slice_in_dim(cells, 0, width, axis=2)
    tail = lax.slice_in_dim(cells, rows - width, rows, axis=2)
    above = lax.ppermute(tail, "space", [(i, i + 1) for i in range(ends)])
    below = lax.ppermute(head, "space", [(i + 1, i) for i in range(ends)])
    return jnp.concatenate([above, cells, below], axis=2)


def pad_depth_cols(field):
    return jnp.pad(field, ((0, 0), (1, 1), (0, 0), (1, 1), (0, 0)))


def conv(padded, kernel):
    return lax.conv_general_dilated(
        padded, kernel, (1, 1, 1), "VALID", dimension_numbers=SPATIAL,
        preferred_element_type=jnp.float32,
    )


def weight_grad(padded, back):
    out = lax.conv_general_dilated(
        padded, back, (1, 1, 1), "VALID", dimension_numbers=("CDHWN", "IDHWO", "NDHWC"),
        preferred_element_type=jnp.float32,
    )
    return out.reshape(out.shape[0], 27, out.shape[4])


def gather_kernel(weight, issued=None):
    count = lax.axis_size("dp")
    local = weight.astype(jnp.bfloat16)
    copies = jnp.broadcast_to(local[None], (count,) + local.shape)
    if issued is not None:
        copies, issued = lax.optimization_barrier((copies, issued))
    full = lax.all_to_all(copies, "dp", 0, 0).reshape((-1,) + local.shape[1:])
    channel = full.shape[0]
    forward = jnp.transpose(full.reshape(channel, 3, 3, 3, full.shape[2]), (1, 2, 3, 0, 4))
    backward = jnp.transpose(forward[::-1, ::-1, ::-1], (0, 1, 2, 4, 3))
    if issued is not None:
        return forward, backward, issued
    return forward, backward


def reduce_grads(grads):
    count = lax.axis_size("dp")
    size = lax.axis_size("space")
    me = lax.axis_index("space")
    core = me % 2
    rows = grads[0].shape[0] // count
    parts = jnp.stack([g.reshape((count, 2, rows // 2) + g.shape[1:]) for g in grads], axis=1)
    keep = lax.dynamic_index_in_dim(parts, core, axis=2, keepdims=False)
    send = lax.dynamic_index_in_dim(parts, 1 - core, axis=2, keepdims=False)
    mine = keep + lax.ppermute(send, "space", [(i, i ^ 1) for i in range(size)])
    owned = lax.all_to_all(mine.astype(jnp.bfloat16), "dp", 0, 0).astype(jnp.float32).sum(axis=0)
    pairs = size // 2
    pieces = owned.reshape(pairs, -1)
    length = pieces.shape[1]
    tiled = -(-length // 1024) * 1024
    pieces = jnp.pad(pieces, ((0, 0), (0, tiled - length))).reshape(pairs, tiled // 128, 128)
    spread = jnp.repeat(pieces, 2, axis=0)
    got = lax.all_to_all(spread, "space", 0, 0).reshape(pairs, 2, tiled // 128, 128)
    piece = lax.dynamic_index_in_dim(got, core, axis=1, keepdims=False).sum(axis=0)
    copies = jnp.broadcast_to(piece[None], (size,) + piece.shape)
    full = lax.all_to_all(copies, "space", 0, 0).reshape(pairs, 2, tiled)[:, :, :length]
    halves = jnp.transpose(full, (1, 0, 2)).reshape((2,) + owned.shape)
    joined = jnp.transpose(halves, (1, 0, 2, 3, 4)).reshape((len(grads), rows) + grads[0].shape[1:])
    return [joined[i] for i in range(len(grads))]


def on_device(inputs, land_mask, weight_one, weight_two, cotangent):
    rows = inputs.shape[2]
    channel = inputs.shape[4]
    mask = land_mask.astype(jnp.bfloat16)[..., None]
    back_two = (cotangent.astype(jnp.float32) * mask.astype(jnp.float32)).astype(jnp.bfloat16)
    k1, k1_t, (rimmed, mask) = gather_kernel(weight_one, (jnp.concatenate([inputs, back_two], axis=4), mask))
    both = exchange_rows(rimmed, HALO)
    mask_wide = exchange_rows(mask, HALO).astype(jnp.float32)
    in_wide = both[..., :channel]
    back_two_wide = both[..., channel:]
    mask_mid = mask_wide[:, :, 1 : rows + 3]
    mask_own = mask_wide[:, :, 2 : rows + 2]

    k2, k2_t = gather_kernel(weight_two)

    pre_one = conv(pad_depth_cols(in_wide), k1)
    sigma = jax.nn.sigmoid(pre_one)
    act_one = (mask_mid * (pre_one * sigma)).astype(jnp.bfloat16)
    act_pad = pad_depth_cols(act_one)
    prediction = (mask_own * conv(act_pad, k2)).astype(jnp.bfloat16)

    back_own = back_two_wide[:, :, HALO : HALO + rows]
    grad_two_terms = weight_grad(act_pad, back_own)
    grad_two_terms, back_two_wide = lax.optimization_barrier((grad_two_terms, back_two_wide))

    pull_one = conv(pad_depth_cols(back_two_wide), k2_t)
    back_one = (pull_one * mask_mid * sigma * (1.0 + pre_one * (1.0 - sigma))).astype(jnp.bfloat16)
    in_mid = pad_depth_cols(in_wide[:, :, 1 : rows + 3])
    grad_one_terms = weight_grad(in_mid, back_one[:, :, 1 : rows + 1])
    grad_one, grad_two = reduce_grads([grad_one_terms, grad_two_terms])
    input_grad = conv(pad_depth_cols(back_one), k1_t).astype(jnp.bfloat16)
    return (prediction, input_grad, grad_one, grad_two)


def solution(mesh):
    in_specs = (
        P("dp", None, "space", None, None),
        P("dp", None, "space", None),
        P("dp", None, None),
        P("dp", None, None),
        P("dp", None, "space", None, None),
    )
    out_specs = (
        P("dp", None, "space", None, None),
        P("dp", None, "space", None, None),
        P("dp", None, None),
        P("dp", None, None),
    )
    return jax.shard_map(
        on_device, mesh=mesh, in_specs=in_specs, out_specs=out_specs, check_vma=False
    )
```

```python
import jax
import jax.numpy as jnp
from jax import lax
from jax.sharding import PartitionSpec as P

HALO = 2
SPATIAL = ("NDHWC", "DHWIO", "NDHWC")


def exchange_rows(cells, width):
    count = lax.axis_size("space")
    ends = count - 1
    rows = cells.shape[2]
    head = lax.slice_in_dim(cells, 0, width, axis=2)
    tail = lax.slice_in_dim(cells, rows - width, rows, axis=2)
    above = lax.ppermute(tail, "space", [(i, i + 1) for i in range(ends)])
    below = lax.ppermute(head, "space", [(i + 1, i) for i in range(ends)])
    return jnp.concatenate([above, cells, below], axis=2)


def pad_depth_cols(field):
    return jnp.pad(field, ((0, 0), (1, 1), (0, 0), (1, 1), (0, 0)))


def conv(padded, kernel):
    return lax.conv_general_dilated(
        padded, kernel, (1, 1, 1), "VALID", dimension_numbers=SPATIAL,
        preferred_element_type=jnp.float32,
    )


def weight_grad(padded, back):
    out = lax.conv_general_dilated(
        padded, back, (1, 1, 1), "VALID", dimension_numbers=("CDHWN", "IDHWO", "NDHWC"),
        preferred_element_type=jnp.float32,
    )
    return out.reshape(out.shape[0], 27, out.shape[4])


def gather_kernel(weight, issued=None):
    count = lax.axis_size("dp")
    local = weight.astype(jnp.bfloat16)
    copies = jnp.broadcast_to(local[None], (count,) + local.shape)
    if issued is not None:
        copies, issued = lax.optimization_barrier((copies, issued))
    full = lax.all_to_all(copies, "dp", 0, 0).reshape((-1,) + local.shape[1:])
    channel = full.shape[0]
    forward = jnp.transpose(full.reshape(channel, 3, 3, 3, full.shape[2]), (1, 2, 3, 0, 4))
    backward = jnp.transpose(forward[::-1, ::-1, ::-1], (0, 1, 2, 4, 3))
    if issued is not None:
        return forward, backward, issued
    return forward, backward


def reduce_grads(grads):
    count = lax.axis_size("dp")
    size = lax.axis_size("space")
    me = lax.axis_index("space")
    core = me % 2
    rows = grads[0].shape[0] // count
    parts = jnp.stack([g.reshape((count, 2, rows // 2) + g.shape[1:]) for g in grads], axis=1)
    keep = lax.dynamic_index_in_dim(parts, core, axis=2, keepdims=False)
    send = lax.dynamic_index_in_dim(parts, 1 - core, axis=2, keepdims=False)
    other = lax.ppermute(send.astype(jnp.bfloat16), "space", [(i, i ^ 1) for i in range(size)])
    mine = keep + other.astype(jnp.float32)
    owned = lax.all_to_all(mine.astype(jnp.bfloat16), "dp", 0, 0).astype(jnp.float32).sum(axis=0)
    pairs = size // 2
    pieces = owned.reshape(pairs, -1)
    length = pieces.shape[1]
    tiled = -(-length // 1024) * 1024
    pieces = jnp.pad(pieces, ((0, 0), (0, tiled - length))).reshape(pairs, tiled // 128, 128)
    spread = jnp.repeat(pieces, 2, axis=0)
    got = lax.all_to_all(spread, "space", 0, 0).reshape(pairs, 2, tiled // 128, 128)
    piece = lax.dynamic_index_in_dim(got, core, axis=1, keepdims=False).sum(axis=0)
    copies = jnp.broadcast_to(piece[None], (size,) + piece.shape)
    full = lax.all_to_all(copies, "space", 0, 0).reshape(pairs, 2, tiled)[:, :, :length]
    halves = jnp.transpose(full, (1, 0, 2)).reshape((2,) + owned.shape)
    joined = jnp.transpose(halves, (1, 0, 2, 3, 4)).reshape((len(grads), rows) + grads[0].shape[1:])
    return [joined[i] for i in range(len(grads))]


def on_device(inputs, land_mask, weight_one, weight_two, cotangent):
    rows = inputs.shape[2]
    channel = inputs.shape[4]
    mask = land_mask.astype(jnp.bfloat16)[..., None]
    back_two = (cotangent.astype(jnp.float32) * mask.astype(jnp.float32)).astype(jnp.bfloat16)
    k1, k1_t, (rimmed, mask) = gather_kernel(weight_one, (jnp.concatenate([inputs, back_two], axis=4), mask))
    both = exchange_rows(rimmed, HALO)
    mask_wide = exchange_rows(mask, HALO).astype(jnp.float32)
    in_wide = both[..., :channel]
    back_two_wide = both[..., channel:]
    mask_mid = mask_wide[:, :, 1 : rows + 3]
    mask_own = mask_wide[:, :, 2 : rows + 2]

    k2, k2_t = gather_kernel(weight_two)

    pre_one = conv(pad_depth_cols(in_wide), k1)
    sigma = jax.nn.sigmoid(pre_one)
    act_one = (mask_mid * (pre_one * sigma)).astype(jnp.bfloat16)
    act_pad = pad_depth_cols(act_one)
    prediction = (mask_own * conv(act_pad, k2)).astype(jnp.bfloat16)

    back_own = back_two_wide[:, :, HALO : HALO + rows]
    grad_two_terms = weight_grad(act_pad, back_own)
    grad_two_terms, back_two_wide = lax.optimization_barrier((grad_two_terms, back_two_wide))

    pull_one = conv(pad_depth_cols(back_two_wide), k2_t)
    back_one = (pull_one * mask_mid * sigma * (1.0 + pre_one * (1.0 - sigma))).astype(jnp.bfloat16)
    in_mid = pad_depth_cols(in_wide[:, :, 1 : rows + 3])
    grad_one_terms = weight_grad(in_mid, back_one[:, :, 1 : rows + 1])
    grad_one, grad_two = reduce_grads([grad_one_terms, grad_two_terms])
    input_grad = conv(pad_depth_cols(back_one), k1_t).astype(jnp.bfloat16)
    return (prediction, input_grad, grad_one, grad_two)


def solution(mesh):
    in_specs = (
        P("dp", None, "space", None, None),
        P("dp", None, "space", None),
        P("dp", None, None),
        P("dp", None, None),
        P("dp", None, "space", None, None),
    )
    out_specs = (
        P("dp", None, "space", None, None),
        P("dp", None, "space", None, None),
        P("dp", None, None),
        P("dp", None, None),
    )
    return jax.shard_map(
        on_device, mesh=mesh, in_specs=in_specs, out_specs=out_specs, check_vma=False
    )
```
